32 devices in a mesh: grid: 4 (over z), mode: 8 (over y, x, core).
Axes of the slice: x: 2, y: 2, z: 4, core: 2. Of those that a mesh axis runs over, the one named last changes fastest.
Arguments:
- modes_field: bfloat16 [512, 192, 1024], P('mode', 'grid'), may hold values from -6 to 6
- chaos_basis: bfloat16 [512, 512], replicated, may hold values from -0.25 to 0.25
- node_weights: float32 [512], replicated, may hold values from 0.5 to 2
- node_points: float32 [512, 16], replicated, may hold values from -4 to 4
- kl_fields: float32 [16, 192, 1024], P(None, 'grid'), may hold values from -0.6 to 0.6
- velocity: float32 [2, 192, 1024], P(None, 'grid'), may hold values from -4 to 4
Outputs:
- tendency: bfloat16 [512, 192, 1024], P('mode', 'grid')
The draws below stay inside these ranges and needn't reach their ends.
All inputs are finite; a program needn't handle non-finite values.
Results may differ from the reference program's by a relative error of at most 0.0053.
Values may be sent and summed in bfloat16 or wider, within the bound.
No kernel may reach another device: no remote copies, remote signals or barrier semaphores. Data moves between devices by JAX's collectives and lax.ppermute only.
A program may use at most 128 MiB of HBM per device.

```python
import math
import jax
import jax.numpy as jnp
from jax import lax

MODES = 512
NODES = 512
TERMS = 16
ROWS = 48
NX = 192
NY = 1024
N_GRID = 4


def block_levels(own_key, shape, split, least, largest):
    loudness, own = 1.0, jax.random.fold_in(own_key, 6)
    for position, parts in split:
        draws = jnp.exp(jax.random.uniform(jax.random.fold_in(own, position), (parts,), jnp.float32, least / len(split), largest / len(split)))
        loudness = loudness * jnp.repeat(draws, shape[position] // parts).reshape([-1 if axis == position else 1 for axis in range(len(shape))])
    return loudness


def normal_values(key, dims, deviation, limit, pieces=(), kind=jnp.bfloat16):
    values = jax.random.normal(key, dims, jnp.float32) * deviation
    if len(pieces) > 0:
        values = block_levels(key, dims, pieces, -0.22, 0.18) * values
    return jnp.clip(values, min=-limit, max=limit).astype(kind)


def setup_inputs(seed: int = 0) -> dict:
    seeds = jax.random.split(jax.random.key(seed), 7)
    return {
        "modes_field": normal_values(seeds[0], (MODES, NX, NY), 1.0, 6.0, ((0, 8), (1, 4))),
        "chaos_basis": normal_values(seeds[1], (NODES, MODES), MODES ** -0.5, 0.25),
        "node_weights": jnp.clip(jnp.exp(jax.random.uniform(seeds[2], (NODES,), jnp.float32, math.log(0.5), math.log(2.0))), 0.5, 2.0),
        "node_points": normal_values(seeds[3], (NODES, TERMS), 1.0, 4.0, (), jnp.float32),
        "kl_fields": normal_values(seeds[4], (TERMS, NX, NY), 0.15, 0.6, ((1, 4),), jnp.float32),
        "velocity": normal_values(seeds[5], (2, NX, NY), 1.0, 4.0, ((1, 4),), jnp.float32),
    }


def node_terms(padded_field, kl_piece, node_points, velocity_piece, node_weights):
    field_value = padded_field.astype(jnp.float32)
    viscosity = jnp.exp(jnp.einsum("qk,krc->qrc", node_points, kl_piece, precision=lax.Precision.HIGHEST))
    center = field_value[:, 1:-1, 1:-1]
    visc_center = viscosity[:, 1:-1, 1:-1]

    def face_flux(near_field, near_visc):
        return 0.5 * (visc_center + near_visc) * (near_field - center)

    north = field_value[:, 2:, 1:-1]
    south = field_value[:, :-2, 1:-1]
    east = field_value[:, 1:-1, 2:]
    west = field_value[:, 1:-1, :-2]
    diffusion = face_flux(north, viscosity[:, 2:, 1:-1]) + face_flux(south, viscosity[:, :-2, 1:-1])
    diffusion = diffusion + face_flux(east, viscosity[:, 1:-1, 2:]) + face_flux(west, viscosity[:, 1:-1, :-2])
    advection = 0.5 * velocity_piece[0] * (north - south) + 0.5 * velocity_piece[1] * (east - west)
    flux = diffusion - advection
    return (node_weights[:, None, None] * flux).astype(jnp.bfloat16)


def reference(modes_field, chaos_basis, node_weights, node_points, kl_fields, velocity):
    modes_padded = jnp.pad(modes_field, ((0, 0), (1, 1), (0, 0)))
    kl_padded = jnp.pad(kl_fields, ((0, 0), (1, 1), (1, 1)))

    def one_block(block_index):
        row_start = (block_index * ROWS).astype(jnp.int32)
        row_piece = lax.dynamic_slice_in_dim(modes_padded, row_start, ROWS + 2, 1)
        nodal = jnp.dot(chaos_basis, row_piece.reshape(MODES, -1), preferred_element_type=jnp.float32)
        nodal = nodal.astype(jnp.bfloat16).reshape(NODES, ROWS + 2, NY)
        padded_field = jnp.pad(nodal, ((0, 0), (0, 0), (1, 1)))
        kl_piece = lax.dynamic_slice_in_dim(kl_padded, row_start, ROWS + 2, 1)
        velocity_piece = lax.dynamic_slice_in_dim(velocity, row_start, ROWS, 1)
        weighted = node_terms(padded_field, kl_piece, node_points, velocity_piece, node_weights)
        tendency = jnp.dot(chaos_basis.T, weighted.reshape(NODES, -1), preferred_element_type=jnp.float32)
        return tendency.astype(jnp.bfloat16).reshape(MODES, ROWS, NY)

    blocks = lax.map(one_block, jnp.arange(N_GRID, dtype=jnp.int32))
    return jnp.transpose(blocks, (1, 0, 2, 3)).reshape(MODES, NX, NY)
```

```python
import jax
import jax.numpy as jnp
from jax import lax
from jax.sharding import PartitionSpec as P


def extended(cells, sides, width):
    for axis, dim in sides:
        count = lax.axis_size(axis)
        ends = count - 1
        head = lax.slice_in_dim(cells, 0, width, axis=dim)
        tail = lax.slice_in_dim(cells, cells.shape[dim] - width, cells.shape[dim], axis=dim)
        cells = jnp.concatenate(
            [
                lax.ppermute(tail, axis, [(i, (i + 1) % count) for i in range(ends)]),
                cells,
                lax.ppermute(head, axis, [((i + 1) % count, i) for i in range(ends)]),
            ],
            axis=dim,
        )
    return cells


def node_terms(padded_field, kl_piece, node_points, velocity_piece, node_weights):
    field_value = padded_field.astype(jnp.float32)
    viscosity = jnp.exp(
        jnp.einsum("qk,krc->qrc", node_points, kl_piece, precision=lax.Precision.HIGHEST)
    )
    center = field_value[:, 1:-1, 1:-1]
    visc_center = viscosity[:, 1:-1, 1:-1]

    def face_flux(near_field, near_visc):
        return 0.5 * (visc_center + near_visc) * (near_field - center)

    north = field_value[:, 2:, 1:-1]
    south = field_value[:, :-2, 1:-1]
    east = field_value[:, 1:-1, 2:]
    west = field_value[:, 1:-1, :-2]
    diffusion = face_flux(north, viscosity[:, 2:, 1:-1]) + face_flux(south, viscosity[:, :-2, 1:-1])
    diffusion = (
        diffusion
        + face_flux(east, viscosity[:, 1:-1, 2:])
        + face_flux(west, viscosity[:, 1:-1, :-2])
    )
    advection = 0.5 * velocity_piece[0] * (north - south) + 0.5 * velocity_piece[1] * (east - west)
    flux = diffusion - advection
    return (node_weights[:, None, None] * flux).astype(jnp.bfloat16)


def local(modes_field, chaos_basis, node_weights, node_points, kl_fields, velocity):
    columns = modes_field.shape[2] // lax.axis_size("mode")
    first_column = lax.axis_index("mode") * columns
    kl_rimmed = extended(kl_fields, (("grid", 1),), 1)
    kl_rimmed = jnp.pad(kl_rimmed, ((0, 0), (0, 0), (1, 1)))
    kl_piece = lax.dynamic_slice_in_dim(kl_rimmed, first_column, columns + 2, 2)
    velocity_piece = lax.dynamic_slice_in_dim(velocity, first_column, columns, 2)
    result = jnp.einsum(
        "qp,prc->qrc",
        chaos_basis,
        lax.all_to_all(modes_field, "mode", split_axis=2, concat_axis=0, tiled=True),
        preferred_element_type=jnp.float32,
    )
    nodal = result.astype(jnp.bfloat16)
    padded_field = extended(nodal, (("mode", 2), ("grid", 1)), 1)
    weighted = node_terms(padded_field, kl_piece, node_points, velocity_piece, node_weights)
    tendency = jnp.einsum(
        "qp,qrc->prc", chaos_basis, weighted, preferred_element_type=jnp.float32
    )
    tendency = tendency.astype(jnp.bfloat16)
    return lax.all_to_all(tendency, "mode", split_axis=0, concat_axis=2, tiled=True)


def solution(mesh):
    return jax.shard_map(
        local,
        mesh=mesh,
        in_specs=(
            P("mode", "grid", None),
            P(),
            P(),
            P(),
            P(None, "grid", None),
            P(None, "grid", None),
        ),
        out_specs=P("mode", "grid", None),
        check_vma=False,
    )
```

```python
import jax
import jax.numpy as jnp
from jax import lax
from jax.sharding import PartitionSpec as P


def extended(cells, sides, width):
    for axis, dim in sides:
        count = lax.axis_size(axis)
        ends = count - 1
        head = lax.slice_in_dim(cells, 0, width, axis=dim)
        tail = lax.slice_in_dim(cells, cells.shape[dim] - width, cells.shape[dim], axis=dim)
        cells = jnp.concatenate(
            [
                lax.ppermute(tail, axis, [(i, (i + 1) % count) for i in range(ends)]),
                cells,
                lax.ppermute(head, axis, [((i + 1) % count, i) for i in range(ends)]),
            ],
            axis=dim,
        )
    return cells


def node_terms(padded_field, kl_piece, node_points, velocity_piece, node_weights):
    field_value = padded_field.astype(jnp.float32)
    viscosity = jnp.exp(
        jnp.einsum("qk,krc->qrc", node_points, kl_piece, precision=lax.Precision.HIGHEST)
    )
    center = field_value[:, 1:-1, 1:-1]
    visc_center = viscosity[:, 1:-1, 1:-1]

    def face_flux(near_field, near_visc):
        return 0.5 * (visc_center + near_visc) * (near_field - center)

    north = field_value[:, 2:, 1:-1]
    south = field_value[:, :-2, 1:-1]
    east = field_value[:, 1:-1, 2:]
    west = field_value[:, 1:-1, :-2]
    diffusion = face_flux(north, viscosity[:, 2:, 1:-1]) + face_flux(south, viscosity[:, :-2, 1:-1])
    diffusion = (
        diffusion
        + face_flux(east, viscosity[:, 1:-1, 2:])
        + face_flux(west, viscosity[:, 1:-1, :-2])
    )
    advection = 0.5 * velocity_piece[0] * (north - south) + 0.5 * velocity_piece[1] * (east - west)
    flux = diffusion - advection
    return (node_weights[:, None, None] * flux).astype(jnp.bfloat16)


def local(modes_field, chaos_basis, node_weights, node_points, kl_fields, velocity):
    parts = lax.axis_size("mode")
    share, rows, width = modes_field.shape
    columns = width // parts
    first_column = lax.axis_index("mode") * columns
    kl_rimmed = extended(kl_fields, (("grid", 1),), 1)
    kl_rimmed = jnp.pad(kl_rimmed, ((0, 0), (0, 0), (1, 1)))
    kl_piece = lax.dynamic_slice_in_dim(kl_rimmed, first_column, columns + 2, 2)
    velocity_piece = lax.dynamic_slice_in_dim(velocity, first_column, columns, 2)
    modes_rimmed = extended(modes_field, (("grid", 1),), 1)
    outgoing = modes_rimmed.reshape(share, rows + 2, parts, columns).transpose(2, 0, 1, 3)
    outgoing = outgoing.reshape(parts, share, (rows + 2) * columns)
    incoming = lax.all_to_all(outgoing, "mode", split_axis=0, concat_axis=0, tiled=True)
    incoming = incoming.reshape(parts * share, (rows + 2) * columns)
    nodal = jnp.dot(chaos_basis, incoming, preferred_element_type=jnp.float32)
    nodal = nodal.astype(jnp.bfloat16).reshape(-1, rows + 2, columns)
    padded_field = extended(nodal, (("mode", 2),), 1)
    weighted = node_terms(padded_field, kl_piece, node_points, velocity_piece, node_weights)
    tendency = jnp.dot(
        chaos_basis.T, weighted.reshape(-1, rows * columns), preferred_element_type=jnp.float32
    )
    tendency = tendency.astype(jnp.bfloat16).reshape(parts, share, rows * columns)
    back = lax.all_to_all(tendency, "mode", split_axis=0, concat_axis=0, tiled=True)
    back = back.reshape(parts, share, rows, columns).transpose(1, 2, 0, 3)
    return back.reshape(share, rows, width)


def solution(mesh):
    return jax.shard_map(
        local,
        mesh=mesh,
        in_specs=(
            P("mode", "grid", None),
            P(),
            P(),
            P(),
            P(None, "grid", None),
            P(None, "grid", None),
        ),
        out_specs=P("mode", "grid", None),
        check_vma=False,
    )
```

```python
import jax
import jax.numpy as jnp
from jax import lax
from jax.sharding import PartitionSpec as P


def extended(cells, sides, width):
    for axis, dim in sides:
        count = lax.axis_size(axis)
        ends = count - 1
        head = lax.slice_in_dim(cells, 0, width, axis=dim)
        tail = lax.slice_in_dim(cells, cells.shape[dim] - width, cells.shape[dim], axis=dim)
        cells = jnp.concatenate(
            [
                lax.ppermute(tail, axis, [(i, (i + 1) % count) for i in range(ends)]),
                cells,
                lax.ppermute(head, axis, [((i + 1) % count, i) for i in range(ends)]),
            ],
            axis=dim,
        )
    return cells


def node_terms(padded_field, kl_piece, node_points, velocity_piece, node_weights):
    field_value = padded_field.astype(jnp.float32)
    viscosity = jnp.exp(
        jnp.einsum("qk,krc->qrc", node_points, kl_piece, precision=lax.Precision.HIGHEST)
    )
    center = field_value[:, 1:-1, 1:-1]
    visc_center = viscosity[:, 1:-1, 1:-1]

    def face_flux(near_field, near_visc):
        return 0.5 * (visc_center + near_visc) * (near_field - center)

    north = field_value[:, 2:, 1:-1]
    south = field_value[:, :-2, 1:-1]
    east = field_value[:, 1:-1, 2:]
    west = field_value[:, 1:-1, :-2]
    diffusion = face_flux(north, viscosity[:, 2:, 1:-1]) + face_flux(south, viscosity[:, :-2, 1:-1])
    diffusion = (
        diffusion
        + face_flux(east, viscosity[:, 1:-1, 2:])
        + face_flux(west, viscosity[:, 1:-1, :-2])
    )
    advection = 0.5 * velocity_piece[0] * (north - south) + 0.5 * velocity_piece[1] * (east - west)
    flux = diffusion - advection
    return (node_weights[:, None, None] * flux).astype(jnp.bfloat16)


CHUNKS = 2


def column_chunk(modes_rimmed, first, rows, parts, columns):
    piece = lax.slice_in_dim(modes_rimmed, first, first + rows + 2, axis=1)
    share = piece.shape[0]
    outgoing = piece.reshape(share, rows + 2, parts, columns).transpose(2, 0, 1, 3)
    return outgoing.reshape(parts, share, (rows + 2) * columns)


def local(modes_field, chaos_basis, node_weights, node_points, kl_fields, velocity):
    parts = lax.axis_size("mode")
    share, rows, width = modes_field.shape
    columns = width // parts
    step = rows // CHUNKS
    first_column = lax.axis_index("mode") * columns
    kl_rimmed = extended(kl_fields, (("grid", 1),), 1)
    kl_rimmed = jnp.pad(kl_rimmed, ((0, 0), (0, 0), (1, 1)))
    kl_rimmed = lax.dynamic_slice_in_dim(kl_rimmed, first_column, columns + 2, 2)
    velocity_piece = lax.dynamic_slice_in_dim(velocity, first_column, columns, 2)
    modes_rimmed = extended(modes_field, (("grid", 1),), 1)
    results = []
    for chunk in range(CHUNKS):
        first = chunk * step
        outgoing = column_chunk(modes_rimmed, first, step, parts, columns)
        incoming = lax.all_to_all(outgoing, "mode", split_axis=0, concat_axis=0, tiled=True)
        incoming = incoming.reshape(parts * share, (step + 2) * columns)
        nodal = jnp.dot(chaos_basis, incoming, preferred_element_type=jnp.float32)
        nodal = nodal.astype(jnp.bfloat16).reshape(-1, step + 2, columns)
        padded_field = extended(nodal, (("mode", 2),), 1)
        kl_piece = lax.slice_in_dim(kl_rimmed, first, first + step + 2, axis=1)
        velocity_rows = lax.slice_in_dim(velocity_piece, first, first + step, axis=1)
        weighted = node_terms(padded_field, kl_piece, node_points, velocity_rows, node_weights)
        tendency = jnp.dot(
            chaos_basis.T, weighted.reshape(-1, step * columns), preferred_element_type=jnp.float32
        )
        tendency = tendency.astype(jnp.bfloat16).reshape(parts, share, step * columns)
        back = lax.all_to_all(tendency, "mode", split_axis=0, concat_axis=0, tiled=True)
        back = back.reshape(parts, share, step, columns).transpose(1, 2, 0, 3)
        results.append(back.reshape(share, step, width))
    return jnp.concatenate(results, axis=1)


def solution(mesh):
    return jax.shard_map(
        local,
        mesh=mesh,
        in_specs=(
            P("mode", "grid", None),
            P(),
            P(),
            P(),
            P(None, "grid", None),
            P(None, "grid", None),
        ),
        out_specs=P("mode", "grid", None),
        check_vma=False,
    )
```

```python
import jax
import jax.numpy as jnp
from jax import lax
from jax.sharding import PartitionSpec as P


def extended(cells, sides, width):
    for axis, dim in sides:
        count = lax.axis_size(axis)
        ends = count - 1
        head = lax.slice_in_dim(cells, 0, width, axis=dim)
        tail = lax.slice_in_dim(cells, cells.shape[dim] - width, cells.shape[dim], axis=dim)
        cells = jnp.concatenate(
            [
                lax.ppermute(tail, axis, [(i, (i + 1) % count) for i in range(ends)]),
                cells,
                lax.ppermute(head, axis, [((i + 1) % count, i) for i in range(ends)]),
            ],
            axis=dim,
        )
    return cells


def node_terms(padded_field, viscosity, velocity_piece, node_weights):
    field_value = padded_field.astype(jnp.float32)
    center = field_value[:, 1:-1, 1:-1]
    visc_center = viscosity[:, 1:-1, 1:-1]

    def face_flux(near_field, near_visc):
        return 0.5 * (visc_center + near_visc) * (near_field - center)

    north = field_value[:, 2:, 1:-1]
    south = field_value[:, :-2, 1:-1]
    east = field_value[:, 1:-1, 2:]
    west = field_value[:, 1:-1, :-2]
    diffusion = face_flux(north, viscosity[:, 2:, 1:-1]) + face_flux(south, viscosity[:, :-2, 1:-1])
    diffusion = (
        diffusion
        + face_flux(east, viscosity[:, 1:-1, 2:])
        + face_flux(west, viscosity[:, 1:-1, :-2])
    )
    advection = 0.5 * velocity_piece[0] * (north - south) + 0.5 * velocity_piece[1] * (east - west)
    flux = diffusion - advection
    return (node_weights[:, None, None] * flux).astype(jnp.bfloat16)


CHUNKS = 2


def column_chunk(modes_rimmed, first, rows, parts, columns):
    piece = lax.slice_in_dim(modes_rimmed, first, first + rows + 2, axis=1)
    share = piece.shape[0]
    outgoing = piece.reshape(share, rows + 2, parts, columns).transpose(2, 0, 1, 3)
    return outgoing.reshape(parts, share, (rows + 2) * columns)


def local(modes_field, chaos_basis, node_weights, node_points, kl_fields, velocity):
    parts = lax.axis_size("mode")
    share, rows, width = modes_field.shape
    columns = width // parts
    step = rows // CHUNKS
    first_column = lax.axis_index("mode") * columns
    modes_rimmed = extended(modes_field, (("grid", 1),), 1)
    outgoing = [
        column_chunk(modes_rimmed, chunk * step, step, parts, columns) for chunk in range(CHUNKS)
    ]
    incoming = lax.all_to_all(outgoing[0], "mode", split_axis=0, concat_axis=0, tiled=True)
    kl_rimmed = extended(kl_fields, (("grid", 1),), 1)
    kl_rimmed = jnp.pad(kl_rimmed, ((0, 0), (0, 0), (1, 1)))
    kl_rimmed = lax.dynamic_slice_in_dim(kl_rimmed, first_column, columns + 2, 2)
    velocity_piece = lax.dynamic_slice_in_dim(velocity, first_column, columns, 2)
    viscosity = jnp.exp(
        jnp.einsum("qk,krc->qrc", node_points, kl_rimmed, precision=lax.Precision.HIGHEST)
    )
    viscosity, later = lax.optimization_barrier((viscosity, outgoing[1:]))
    outgoing = outgoing[:1] + list(later)
    results = []
    for chunk in range(CHUNKS):
        first = chunk * step
        if chunk > 0:
            incoming = lax.all_to_all(outgoing[chunk], "mode", split_axis=0, concat_axis=0, tiled=True)
            incoming, tendency = lax.optimization_barrier((incoming, tendency))
            back = lax.all_to_all(tendency, "mode", split_axis=0, concat_axis=0, tiled=True)
            back = back.reshape(parts, share, step, columns).transpose(1, 2, 0, 3)
            results.append(back.reshape(share, step, width))
        incoming = incoming.reshape(parts * share, (step + 2) * columns)
        nodal = jnp.dot(chaos_basis, incoming, preferred_element_type=jnp.float32)
        nodal = nodal.astype(jnp.bfloat16).reshape(-1, step + 2, columns)
        padded_field = extended(nodal, (("mode", 2),), 1)
        visc_piece = lax.slice_in_dim(viscosity, first, first + step + 2, axis=1)
        velocity_rows = lax.slice_in_dim(velocity_piece, first, first + step, axis=1)
        weighted = node_terms(padded_field, visc_piece, velocity_rows, node_weights)
        tendency = jnp.dot(
            chaos_basis.T, weighted.reshape(-1, step * columns), preferred_element_type=jnp.float32
        )
        tendency = tendency.astype(jnp.bfloat16).reshape(parts, share, step * columns)
    back = lax.all_to_all(tendency, "mode", split_axis=0, concat_axis=0, tiled=True)
    back = back.reshape(parts, share, step, columns).transpose(1, 2, 0, 3)
    results.append(back.reshape(share, step, width))
    return jnp.concatenate(results, axis=1)


def solution(mesh):
    return jax.shard_map(
        local,
        mesh=mesh,
        in_specs=(
            P("mode", "grid", None),
            P(),
            P(),
            P(),
            P(None, "grid", None),
            P(None, "grid", None),
        ),
        out_specs=P("mode", "grid", None),
        check_vma=False,
    )
```

```python
import jax
import jax.numpy as jnp
from jax import lax
from jax.sharding import PartitionSpec as P


def extended(cells, sides, width):
    for axis, dim in sides:
        count = lax.axis_size(axis)
        ends = count - 1
        head = lax.slice_in_dim(cells, 0, width, axis=dim)
        tail = lax.slice_in_dim(cells, cells.shape[dim] - width, cells.shape[dim], axis=dim)
        cells = jnp.concatenate(
            [
                lax.ppermute(tail, axis, [(i, (i + 1) % count) for i in range(ends)]),
                cells,
                lax.ppermute(head, axis, [((i + 1) % count, i) for i in range(ends)]),
            ],
            axis=dim,
        )
    return cells


def node_terms(padded_field, viscosity, velocity_piece, node_weights):
    field_value = padded_field.astype(jnp.float32)
    center = field_value[:, 1:-1, 1:-1]
    visc_center = viscosity[:, 1:-1, 1:-1]

    def face_flux(near_field, near_visc):
        return 0.5 * (visc_center + near_visc) * (near_field - center)

    north = field_value[:, 2:, 1:-1]
    south = field_value[:, :-2, 1:-1]
    east = field_value[:, 1:-1, 2:]
    west = field_value[:, 1:-1, :-2]
    diffusion = face_flux(north, viscosity[:, 2:, 1:-1]) + face_flux(south, viscosity[:, :-2, 1:-1])
    diffusion = (
        diffusion
        + face_flux(east, viscosity[:, 1:-1, 2:])
        + face_flux(west, viscosity[:, 1:-1, :-2])
    )
    advection = 0.5 * velocity_piece[0] * (north - south) + 0.5 * velocity_piece[1] * (east - west)
    flux = diffusion - advection
    return (node_weights[:, None, None] * flux).astype(jnp.bfloat16)


CHUNKS = 2


def column_chunk(modes_rimmed, first, rows, parts, columns):
    piece = lax.slice_in_dim(modes_rimmed, first, first + rows + 2, axis=1)
    share = piece.shape[0]
    blocks = piece.reshape(share, rows + 2, parts, columns)
    zero = jnp.zeros((share, rows + 2, 1), piece.dtype)
    west = jnp.concatenate([zero, blocks[:, :, :-1, columns - 1]], axis=2)
    east = jnp.concatenate([blocks[:, :, 1:, 0], zero], axis=2)
    rims = jnp.concatenate([west, east], axis=1).transpose(2, 0, 1)
    rims = jnp.pad(rims, ((0, 0), (0, 0), (0, columns - 2 * (rows + 2))))
    outgoing = blocks.transpose(2, 0, 1, 3).reshape(parts, share, (rows + 2) * columns)
    return jnp.concatenate([outgoing, rims], axis=2)


def local(modes_field, chaos_basis, node_weights, node_points, kl_fields, velocity):
    parts = lax.axis_size("mode")
    share, rows, width = modes_field.shape
    columns = width // parts
    step = rows // CHUNKS
    first_column = lax.axis_index("mode") * columns
    modes_rimmed = extended(modes_field, (("grid", 1),), 1)
    outgoing = [
        column_chunk(modes_rimmed, chunk * step, step, parts, columns) for chunk in range(CHUNKS)
    ]
    incoming = lax.all_to_all(outgoing[0], "mode", split_axis=0, concat_axis=0, tiled=True)
    kl_rimmed = extended(kl_fields, (("grid", 1),), 1)
    kl_rimmed = jnp.pad(kl_rimmed, ((0, 0), (0, 0), (1, 1)))
    kl_rimmed = lax.dynamic_slice_in_dim(kl_rimmed, first_column, columns + 2, 2)
    velocity_piece = lax.dynamic_slice_in_dim(velocity, first_column, columns, 2)
    viscosity = jnp.exp(
        jnp.einsum("qk,krc->qrc", node_points, kl_rimmed, precision=lax.Precision.HIGHEST)
    )
    viscosity, later = lax.optimization_barrier((viscosity, outgoing[1:]))
    outgoing = outgoing[:1] + list(later)
    results = []
    body = (step + 2) * columns
    for chunk in range(CHUNKS):
        first = chunk * step
        if chunk > 0:
            incoming = lax.all_to_all(outgoing[chunk], "mode", split_axis=0, concat_axis=0, tiled=True)
            incoming, tendency = lax.optimization_barrier((incoming, tendency))
            back = lax.all_to_all(tendency, "mode", split_axis=0, concat_axis=0, tiled=True)
            back = back.reshape(parts, share, step, columns).transpose(1, 2, 0, 3)
            results.append(back.reshape(share, step, width))
        incoming = incoming.reshape(parts * share, body + columns)
        nodal = jnp.dot(chaos_basis, incoming, preferred_element_type=jnp.float32)
        nodal = nodal.astype(jnp.bfloat16)
        centre = nodal[:, :body].reshape(-1, step + 2, columns)
        west = nodal[:, body : body + step + 2].reshape(-1, step + 2, 1)
        east = nodal[:, body + step + 2 : body + 2 * (step + 2)].reshape(-1, step + 2, 1)
        padded_field = jnp.concatenate([west, centre, east], axis=2)
        visc_piece = lax.slice_in_dim(viscosity, first, first + step + 2, axis=1)
        velocity_rows = lax.slice_in_dim(velocity_piece, first, first + step, axis=1)
        weighted = node_terms(padded_field, visc_piece, velocity_rows, node_weights)
        tendency = jnp.dot(
            chaos_basis.T, weighted.reshape(-1, step * columns), preferred_element_type=jnp.float32
        )
        tendency = tendency.astype(jnp.bfloat16).reshape(parts, share, step * columns)
    back = lax.all_to_all(tendency, "mode", split_axis=0, concat_axis=0, tiled=True)
    back = back.reshape(parts, share, step, columns).transpose(1, 2, 0, 3)
    results.append(back.reshape(share, step, width))
    return jnp.concatenate(results, axis=1)


def solution(mesh):
    return jax.shard_map(
        local,
        mesh=mesh,
        in_specs=(
            P("mode", "grid", None),
            P(),
            P(),
            P(),
            P(None, "grid", None),
            P(None, "grid", None),
        ),
        out_specs=P("mode", "grid", None),
        check_vma=False,
    )
```

```python
import jax
import jax.numpy as jnp
from jax import lax
from jax.sharding import PartitionSpec as P


def extended(cells, sides, width):
    for axis, dim in sides:
        count = lax.axis_size(axis)
        ends = count - 1
        head = lax.slice_in_dim(cells, 0, width, axis=dim)
        tail = lax.slice_in_dim(cells, cells.shape[dim] - width, cells.shape[dim], axis=dim)
        cells = jnp.concatenate(
            [
                lax.ppermute(tail, axis, [(i, (i + 1) % count) for i in range(ends)]),
                cells,
                lax.ppermute(head, axis, [((i + 1) % count, i) for i in range(ends)]),
            ],
            axis=dim,
        )
    return cells


def node_terms(padded_field, viscosity, velocity_piece, node_weights):
    field_value = padded_field.astype(jnp.float32)
    center = field_value[:, 1:-1, 1:-1]
    visc_center = viscosity[:, 1:-1, 1:-1]

    def face_flux(near_field, near_visc):
        return 0.5 * (visc_center + near_visc) * (near_field - center)

    north = field_value[:, 2:, 1:-1]
    south = field_value[:, :-2, 1:-1]
    east = field_value[:, 1:-1, 2:]
    west = field_value[:, 1:-1, :-2]
    diffusion = face_flux(north, viscosity[:, 2:, 1:-1]) + face_flux(south, viscosity[:, :-2, 1:-1])
    diffusion = (
        diffusion
        + face_flux(east, viscosity[:, 1:-1, 2:])
        + face_flux(west, viscosity[:, 1:-1, :-2])
    )
    advection = 0.5 * velocity_piece[0] * (north - south) + 0.5 * velocity_piece[1] * (east - west)
    flux = diffusion - advection
    return (node_weights[:, None, None] * flux).astype(jnp.bfloat16)


CHUNKS = 2


def column_chunk(modes_rimmed, first, rows, parts, columns):
    piece = lax.slice_in_dim(modes_rimmed, first, first + rows + 2, axis=1)
    share = piece.shape[0]
    height = rows + 2
    body = piece.reshape(share, height, parts, columns).transpose(2, 0, 1, 3)
    body = body.reshape(parts, share, height * columns)
    place = lax.broadcasted_iota(jnp.int32, (height * columns, columns), 0)
    lane = lax.broadcasted_iota(jnp.int32, (height * columns, columns), 1)
    pick = ((lane < height) & (place == lane * columns + columns - 1)) | (
        (lane >= height) & (lane < 2 * height) & (place == (lane - height) * columns)
    )
    edges = jnp.dot(
        body.reshape(parts * share, height * columns),
        pick.astype(body.dtype),
        preferred_element_type=jnp.float32,
    ).astype(body.dtype).reshape(parts, share, columns)
    zero = jnp.zeros_like(edges[:1])
    from_left = jnp.concatenate([zero, edges[:-1]], axis=0)
    from_right = jnp.concatenate([edges[1:], zero], axis=0)
    side = lax.broadcasted_iota(jnp.int32, edges.shape, 2)
    rims = jnp.where(side < height, from_left, from_right)
    return jnp.concatenate([body, rims], axis=2)


def local(modes_field, chaos_basis, node_weights, node_points, kl_fields, velocity):
    parts = lax.axis_size("mode")
    share, rows, width = modes_field.shape
    columns = width // parts
    lead = rows * 5 // 12
    sizes = [lead, rows - lead]
    starts = [0, lead]
    first_column = lax.axis_index("mode") * columns
    modes_rimmed = extended(modes_field, (("grid", 1),), 1)
    outgoing = [column_chunk(modes_rimmed, f, n, parts, columns) for f, n in zip(starts, sizes)]
    incoming = lax.all_to_all(outgoing[0], "mode", split_axis=0, concat_axis=0, tiled=True)
    kl_rimmed = extended(kl_fields, (("grid", 1),), 1)
    kl_rimmed = jnp.pad(kl_rimmed, ((0, 0), (0, 0), (1, 1)))
    kl_rimmed = lax.dynamic_slice_in_dim(kl_rimmed, first_column, columns + 2, 2)
    velocity_piece = lax.dynamic_slice_in_dim(velocity, first_column, columns, 2)
    viscosity = jnp.exp(
        jnp.einsum("qk,krc->qrc", node_points, kl_rimmed, precision=lax.Precision.HIGHEST)
    )
    viscosity, later = lax.optimization_barrier((viscosity, outgoing[1:]))
    outgoing = outgoing[:1] + list(later)
    results = []
    for chunk, (first, step) in enumerate(zip(starts, sizes)):
        body = (step + 2) * columns
        if chunk > 0:
            incoming = lax.all_to_all(outgoing[chunk], "mode", split_axis=0, concat_axis=0, tiled=True)
            incoming, tendency = lax.optimization_barrier((incoming, tendency))
            back = lax.all_to_all(tendency, "mode", split_axis=0, concat_axis=0, tiled=True)
            back = back.reshape(parts, share, sizes[chunk - 1], columns).transpose(1, 2, 0, 3)
            results.append(back.reshape(share, sizes[chunk - 1], width))
        incoming = incoming.reshape(parts * share, body + columns)
        nodal = jnp.dot(chaos_basis, incoming, preferred_element_type=jnp.float32)
        nodal = nodal.astype(jnp.bfloat16)
        centre = nodal[:, :body].reshape(-1, step + 2, columns)
        west = nodal[:, body : body + step + 2].reshape(-1, step + 2, 1)
        east = nodal[:, body + step + 2 : body + 2 * (step + 2)].reshape(-1, step + 2, 1)
        padded_field = jnp.concatenate([west, centre, east], axis=2)
        visc_piece = lax.slice_in_dim(viscosity, first, first + step + 2, axis=1)
        velocity_rows = lax.slice_in_dim(velocity_piece, first, first + step, axis=1)
        weighted = node_terms(padded_field, visc_piece, velocity_rows, node_weights)
        tendency = jnp.dot(
            chaos_basis.T, weighted.reshape(-1, step * columns), preferred_element_type=jnp.float32
        )
        tendency = tendency.astype(jnp.bfloat16).reshape(parts, share, step * columns)
    back = lax.all_to_all(tendency, "mode", split_axis=0, concat_axis=0, tiled=True)
    back = back.reshape(parts, share, sizes[-1], columns).transpose(1, 2, 0, 3)
    results.append(back.reshape(share, sizes[-1], width))
    return jnp.concatenate(results, axis=1)


def solution(mesh):
    return jax.shard_map(
        local,
        mesh=mesh,
        in_specs=(
            P("mode", "grid", None),
            P(),
            P(),
            P(),
            P(None, "grid", None),
            P(None, "grid", None),
        ),
        out_specs=P("mode", "grid", None),
        check_vma=False,
    )
```

```python
import jax
import jax.numpy as jnp
from jax import lax
from jax.sharding import PartitionSpec as P


def extended(cells, sides, width):
    for axis, dim in sides:
        count = lax.axis_size(axis)
        ends = count - 1
        head = lax.slice_in_dim(cells, 0, width, axis=dim)
        tail = lax.slice_in_dim(cells, cells.shape[dim] - width, cells.shape[dim], axis=dim)
        cells = jnp.concatenate(
            [
                lax.ppermute(tail, axis, [(i, (i + 1) % count) for i in range(ends)]),
                cells,
                lax.ppermute(head, axis, [((i + 1) % count, i) for i in range(ends)]),
            ],
            axis=dim,
        )
    return cells


def node_terms(padded_field, viscosity, velocity_piece, node_weights):
    field_value = padded_field.astype(jnp.float32)
    center = field_value[:, 1:-1, 1:-1]
    visc_center = viscosity[:, 1:-1, 1:-1]

    def face_flux(near_field, near_visc):
        return 0.5 * (visc_center + near_visc) * (near_field - center)

    north = field_value[:, 2:, 1:-1]
    south = field_value[:, :-2, 1:-1]
    east = field_value[:, 1:-1, 2:]
    west = field_value[:, 1:-1, :-2]
    diffusion = face_flux(north, viscosity[:, 2:, 1:-1]) + face_flux(south, viscosity[:, :-2, 1:-1])
    diffusion = (
        diffusion
        + face_flux(east, viscosity[:, 1:-1, 2:])
        + face_flux(west, viscosity[:, 1:-1, :-2])
    )
    advection = 0.5 * velocity_piece[0] * (north - south) + 0.5 * velocity_piece[1] * (east - west)
    flux = diffusion - advection
    return (node_weights[:, None, None] * flux).astype(jnp.bfloat16)


CHUNKS = 2


def column_chunk(modes_rimmed, first, rows, parts, columns):
    piece = lax.slice_in_dim(modes_rimmed, first, first + rows + 2, axis=1)
    share = piece.shape[0]
    height = rows + 2
    body = piece.reshape(share, height, parts, columns).transpose(2, 0, 1, 3)
    body = body.reshape(parts, share, height * columns)
    place = lax.broadcasted_iota(jnp.int32, (height * columns, columns), 0)
    lane = lax.broadcasted_iota(jnp.int32, (height * columns, columns), 1)
    pick = ((lane < height) & (place == lane * columns + columns - 1)) | (
        (lane >= height) & (lane < 2 * height) & (place == (lane - height) * columns)
    )
    edges = jnp.dot(
        body.reshape(parts * share, height * columns),
        pick.astype(body.dtype),
        preferred_element_type=jnp.float32,
    ).astype(body.dtype).reshape(parts, share, columns)
    zero = jnp.zeros_like(edges[:1])
    from_left = jnp.concatenate([zero, edges[:-1]], axis=0)
    from_right = jnp.concatenate([edges[1:], zero], axis=0)
    side = lax.broadcasted_iota(jnp.int32, edges.shape, 2)
    rims = jnp.where(side < height, from_left, from_right)
    return jnp.concatenate([body, rims], axis=2)


def local(modes_field, chaos_basis, node_weights, node_points, kl_fields, velocity):
    parts = lax.axis_size("mode")
    share, rows, width = modes_field.shape
    columns = width // parts
    lead = rows * 5 // 12
    sizes = [lead, rows - lead]
    starts = [0, lead]
    first_column = lax.axis_index("mode") * columns
    modes_rimmed = extended(modes_field, (("grid", 1),), 1)
    outgoing = [column_chunk(modes_rimmed, f, n, parts, columns) for f, n in zip(starts, sizes)]
    incoming = lax.all_to_all(outgoing[0], "mode", split_axis=0, concat_axis=0, tiled=True)
    kl_rimmed = extended(kl_fields, (("grid", 1),), 1)
    kl_rimmed, incoming = lax.optimization_barrier((kl_rimmed, incoming))
    kl_rimmed = jnp.pad(kl_rimmed, ((0, 0), (0, 0), (1, 1)))
    kl_rimmed = lax.dynamic_slice_in_dim(kl_rimmed, first_column, columns + 2, 2)
    velocity_piece = lax.dynamic_slice_in_dim(velocity, first_column, columns, 2)
    viscosity = jnp.exp(
        jnp.einsum("qk,krc->qrc", node_points, kl_rimmed, precision=lax.Precision.HIGHEST)
    )
    results = []
    for chunk, (first, step) in enumerate(zip(starts, sizes)):
        body = (step + 2) * columns
        if chunk > 0:
            incoming = lax.all_to_all(outgoing[chunk], "mode", split_axis=0, concat_axis=0, tiled=True)
            incoming, tendency = lax.optimization_barrier((incoming, tendency))
            back = lax.all_to_all(tendency, "mode", split_axis=0, concat_axis=0, tiled=True)
            back = back.reshape(parts, share, sizes[chunk - 1], columns).transpose(1, 2, 0, 3)
            results.append(back.reshape(share, sizes[chunk - 1], width))
        incoming = incoming.reshape(parts * share, body + columns)
        nodal = jnp.dot(chaos_basis, incoming, preferred_element_type=jnp.float32)
        nodal = nodal.astype(jnp.bfloat16)
        centre = nodal[:, :body].reshape(-1, step + 2, columns)
        west = nodal[:, body : body + step + 2].reshape(-1, step + 2, 1)
        east = nodal[:, body + step + 2 : body + 2 * (step + 2)].reshape(-1, step + 2, 1)
        padded_field = jnp.concatenate([west, centre, east], axis=2)
        visc_piece = lax.slice_in_dim(viscosity, first, first + step + 2, axis=1)
        velocity_rows = lax.slice_in_dim(velocity_piece, first, first + step, axis=1)
        weighted = node_terms(padded_field, visc_piece, velocity_rows, node_weights)
        tendency = jnp.dot(
            chaos_basis.T, weighted.reshape(-1, step * columns), preferred_element_type=jnp.float32
        )
        tendency = tendency.astype(jnp.bfloat16).reshape(parts, share, step * columns)
    back = lax.all_to_all(tendency, "mode", split_axis=0, concat_axis=0, tiled=True)
    back = back.reshape(parts, share, sizes[-1], columns).transpose(1, 2, 0, 3)
    results.append(back.reshape(share, sizes[-1], width))
    return jnp.concatenate(results, axis=1)


def solution(mesh):
    return jax.shard_map(
        local,
        mesh=mesh,
        in_specs=(
            P("mode", "grid", None),
            P(),
            P(),
            P(),
            P(None, "grid", None),
            P(None, "grid", None),
        ),
        out_specs=P("mode", "grid", None),
        check_vma=False,
    )
```

```python
import jax
import jax.numpy as jnp
from jax import lax
from jax.sharding import PartitionSpec as P


def extended(cells, sides, width):
    for axis, dim in sides:
        count = lax.axis_size(axis)
        ends = count - 1
        head = lax.slice_in_dim(cells, 0, width, axis=dim)
        tail = lax.slice_in_dim(cells, cells.shape[dim] - width, cells.shape[dim], axis=dim)
        cells = jnp.concatenate(
            [
                lax.ppermute(tail, axis, [(i, (i + 1) % count) for i in range(ends)]),
                cells,
                lax.ppermute(head, axis, [((i + 1) % count, i) for i in range(ends)]),
            ],
            axis=dim,
        )
    return cells


def node_terms(padded_field, viscosity, velocity_piece, node_weights):
    field_value = padded_field.astype(jnp.float32)
    center = field_value[:, 1:-1, 1:-1]
    visc_center = viscosity[:, 1:-1, 1:-1]

    def face_flux(near_field, near_visc):
        return 0.5 * (visc_center + near_visc) * (near_field - center)

    north = field_value[:, 2:, 1:-1]
    south = field_value[:, :-2, 1:-1]
    east = field_value[:, 1:-1, 2:]
    west = field_value[:, 1:-1, :-2]
    diffusion = face_flux(north, viscosity[:, 2:, 1:-1]) + face_flux(south, viscosity[:, :-2, 1:-1])
    diffusion = (
        diffusion
        + face_flux(east, viscosity[:, 1:-1, 2:])
        + face_flux(west, viscosity[:, 1:-1, :-2])
    )
    advection = 0.5 * velocity_piece[0] * (north - south) + 0.5 * velocity_piece[1] * (east - west)
    flux = diffusion - advection
    return (node_weights[:, None, None] * flux).astype(jnp.bfloat16)


CHUNKS = 2


def column_chunk(modes_rimmed, first, rows, parts, columns):
    piece = lax.slice_in_dim(modes_rimmed, first, first + rows + 2, axis=1)
    share = piece.shape[0]
    height = rows + 2
    body = piece.reshape(share, height, parts, columns).transpose(2, 0, 1, 3)
    body = body.reshape(parts, share, height * columns)
    place = lax.broadcasted_iota(jnp.int32, (height * columns, columns), 0)
    lane = lax.broadcasted_iota(jnp.int32, (height * columns, columns), 1)
    pick = ((lane < height) & (place == lane * columns + columns - 1)) | (
        (lane >= height) & (lane < 2 * height) & (place == (lane - height) * columns)
    )
    edges = jnp.dot(
        body.reshape(parts * share, height * columns),
        pick.astype(body.dtype),
        preferred_element_type=jnp.float32,
    ).astype(body.dtype).reshape(parts, share, columns)
    zero = jnp.zeros_like(edges[:1])
    from_left = jnp.concatenate([zero, edges[:-1]], axis=0)
    from_right = jnp.concatenate([edges[1:], zero], axis=0)
    side = lax.broadcasted_iota(jnp.int32, edges.shape, 2)
    rims = jnp.where(side < height, from_left, from_right)
    return jnp.concatenate([body, rims], axis=2)


def local(modes_field, chaos_basis, node_weights, node_points, kl_fields, velocity):
    parts = lax.axis_size("mode")
    share, rows, width = modes_field.shape
    columns = width // parts
    lead = rows * 5 // 12
    sizes = [lead, rows - lead]
    starts = [0, lead]
    first_column = lax.axis_index("mode") * columns
    modes_rimmed = extended(modes_field, (("grid", 1),), 1)
    outgoing = [column_chunk(modes_rimmed, f, n, parts, columns) for f, n in zip(starts, sizes)]
    incoming = lax.all_to_all(outgoing[0], "mode", split_axis=0, concat_axis=0, tiled=True)
    kl_fields, incoming = lax.optimization_barrier((kl_fields, incoming))
    kl_rimmed = extended(kl_fields, (("grid", 1),), 1)
    kl_rimmed = jnp.pad(kl_rimmed, ((0, 0), (0, 0), (1, 1)))
    kl_rimmed = lax.dynamic_slice_in_dim(kl_rimmed, first_column, columns + 2, 2)
    velocity_piece = lax.dynamic_slice_in_dim(velocity, first_column, columns, 2)
    viscosity = jnp.exp(
        jnp.einsum("qk,krc->qrc", node_points, kl_rimmed, precision=lax.Precision.HIGHEST)
    )
    results = []
    for chunk, (first, step) in enumerate(zip(starts, sizes)):
        body = (step + 2) * columns
        if chunk > 0:
            incoming = lax.all_to_all(outgoing[chunk], "mode", split_axis=0, concat_axis=0, tiled=True)
            incoming, tendency = lax.optimization_barrier((incoming, tendency))
            back = lax.all_to_all(tendency, "mode", split_axis=0, concat_axis=0, tiled=True)
            back = back.reshape(parts, share, sizes[chunk - 1], columns).transpose(1, 2, 0, 3)
            results.append(back.reshape(share, sizes[chunk - 1], width))
        incoming = incoming.reshape(parts * share, body + columns)
        nodal = jnp.dot(chaos_basis, incoming, preferred_element_type=jnp.float32)
        nodal = nodal.astype(jnp.bfloat16)
        centre = nodal[:, :body].reshape(-1, step + 2, columns)
        west = nodal[:, body : body + step + 2].reshape(-1, step + 2, 1)
        east = nodal[:, body + step + 2 : body + 2 * (step + 2)].reshape(-1, step + 2, 1)
        padded_field = jnp.concatenate([west, centre, east], axis=2)
        visc_piece = lax.slice_in_dim(viscosity, first, first + step + 2, axis=1)
        velocity_rows = lax.slice_in_dim(velocity_piece, first, first + step, axis=1)
        weighted = node_terms(padded_field, visc_piece, velocity_rows, node_weights)
        tendency = jnp.dot(
            chaos_basis.T, weighted.reshape(-1, step * columns), preferred_element_type=jnp.float32
        )
        tendency = tendency.astype(jnp.bfloat16).reshape(parts, share, step * columns)
    back = lax.all_to_all(tendency, "mode", split_axis=0, concat_axis=0, tiled=True)
    back = back.reshape(parts, share, sizes[-1], columns).transpose(1, 2, 0, 3)
    results.append(back.reshape(share, sizes[-1], width))
    return jnp.concatenate(results, axis=1)


def solution(mesh):
    return jax.shard_map(
        local,
        mesh=mesh,
        in_specs=(
            P("mode", "grid", None),
            P(),
            P(),
            P(),
            P(None, "grid", None),
            P(None, "grid", None),
        ),
        out_specs=P("mode", "grid", None),
        check_vma=False,
    )
```

```python
import jax
import jax.numpy as jnp
from jax import lax
from jax.sharding import PartitionSpec as P


def extended(cells, sides, width):
    for axis, dim in sides:
        count = lax.axis_size(axis)
        ends = count - 1
        head = lax.slice_in_dim(cells, 0, width, axis=dim)
        tail = lax.slice_in_dim(cells, cells.shape[dim] - width, cells.shape[dim], axis=dim)
        cells = jnp.concatenate(
            [
                lax.ppermute(tail, axis, [(i, (i + 1) % count) for i in range(ends)]),
                cells,
                lax.ppermute(head, axis, [((i + 1) % count, i) for i in range(ends)]),
            ],
            axis=dim,
        )
    return cells


def node_terms(padded_field, viscosity, velocity_piece, node_weights):
    field_value = padded_field.astype(jnp.float32)
    center = field_value[:, 1:-1, 1:-1]
    visc_center = viscosity[:, 1:-1, 1:-1]

    def face_flux(near_field, near_visc):
        return 0.5 * (visc_center + near_visc) * (near_field - center)

    north = field_value[:, 2:, 1:-1]
    south = field_value[:, :-2, 1:-1]
    east = field_value[:, 1:-1, 2:]
    west = field_value[:, 1:-1, :-2]
    diffusion = face_flux(north, viscosity[:, 2:, 1:-1]) + face_flux(south, viscosity[:, :-2, 1:-1])
    diffusion = (
        diffusion
        + face_flux(east, viscosity[:, 1:-1, 2:])
        + face_flux(west, viscosity[:, 1:-1, :-2])
    )
    advection = 0.5 * velocity_piece[0] * (north - south) + 0.5 * velocity_piece[1] * (east - west)
    flux = diffusion - advection
    return (node_weights[:, None, None] * flux).astype(jnp.bfloat16)


CHUNKS = 2


def column_chunk(modes_rimmed, first, rows, parts, columns):
    piece = lax.slice_in_dim(modes_rimmed, first, first + rows + 2, axis=1)
    share = piece.shape[0]
    height = rows + 2
    body = piece.reshape(share, height, parts, columns).transpose(2, 0, 1, 3)
    body = body.reshape(parts, share, height * columns)
    place = lax.broadcasted_iota(jnp.int32, (height * columns, columns), 0)
    lane = lax.broadcasted_iota(jnp.int32, (height * columns, columns), 1)
    pick = ((lane < height) & (place == lane * columns + columns - 1)) | (
        (lane >= height) & (lane < 2 * height) & (place == (lane - height) * columns)
    )
    edges = jnp.dot(
        body.reshape(parts * share, height * columns),
        pick.astype(body.dtype),
        preferred_element_type=jnp.float32,
    ).astype(body.dtype).reshape(parts, share, columns)
    zero = jnp.zeros_like(edges[:1])
    from_left = jnp.concatenate([zero, edges[:-1]], axis=0)
    from_right = jnp.concatenate([edges[1:], zero], axis=0)
    side = lax.broadcasted_iota(jnp.int32, edges.shape, 2)
    rims = jnp.where(side < height, from_left, from_right)
    return jnp.concatenate([body, rims], axis=2)


def local(modes_field, chaos_basis, node_weights, node_points, kl_fields, velocity):
    parts = lax.axis_size("mode")
    share, rows, width = modes_field.shape
    columns = width // parts
    lead = rows * 5 // 12
    sizes = [lead, rows - lead]
    starts = [0, lead]
    first_column = lax.axis_index("mode") * columns
    modes_rimmed = extended(modes_field, (("grid", 1),), 1)
    outgoing = [column_chunk(modes_rimmed, f, n, parts, columns) for f, n in zip(starts, sizes)]
    incoming = lax.all_to_all(outgoing[0], "mode", split_axis=0, concat_axis=0, tiled=True)
    kl_fields, incoming = lax.optimization_barrier((kl_fields, incoming))
    kl_rimmed = extended(kl_fields, (("grid", 1),), 1)
    kl_rimmed = jnp.pad(kl_rimmed, ((0, 0), (0, 0), (1, 1)))
    kl_rimmed = lax.dynamic_slice_in_dim(kl_rimmed, first_column, columns + 2, 2)
    velocity_piece = lax.dynamic_slice_in_dim(velocity, first_column, columns, 2)
    viscosity = jnp.exp(
        jnp.einsum("qk,krc->qrc", node_points, kl_rimmed, precision=lax.Precision.HIGHEST)
    )
    results = []
    for chunk, (first, step) in enumerate(zip(starts, sizes)):
        body = (step + 2) * columns
        if chunk > 0:
            incoming = lax.all_to_all(outgoing[chunk], "mode", split_axis=0, concat_axis=0, tiled=True)
            incoming, tendency = lax.optimization_barrier((incoming, tendency))
            back = lax.all_to_all(tendency, "mode", split_axis=0, concat_axis=0, tiled=True)
            back = back.reshape(parts, share, sizes[chunk - 1], columns)
            results.append(jnp.concatenate([back[s] for s in range(parts)], axis=2))
        incoming = incoming.reshape(parts * share, body + columns)
        nodal = jnp.dot(chaos_basis, incoming, preferred_element_type=jnp.float32)
        nodal = nodal.astype(jnp.bfloat16)
        centre = nodal[:, :body].reshape(-1, step + 2, columns)
        west = nodal[:, body : body + step + 2].reshape(-1, step + 2, 1)
        east = nodal[:, body + step + 2 : body + 2 * (step + 2)].reshape(-1, step + 2, 1)
        padded_field = jnp.concatenate([west, centre, east], axis=2)
        visc_piece = lax.slice_in_dim(viscosity, first, first + step + 2, axis=1)
        velocity_rows = lax.slice_in_dim(velocity_piece, first, first + step, axis=1)
        weighted = node_terms(padded_field, visc_piece, velocity_rows, node_weights)
        tendency = jnp.dot(
            chaos_basis.T, weighted.reshape(-1, step * columns), preferred_element_type=jnp.float32
        )
        tendency = tendency.astype(jnp.bfloat16).reshape(parts, share, step * columns)
    back = lax.all_to_all(tendency, "mode", split_axis=0, concat_axis=0, tiled=True)
    back = back.reshape(parts, share, sizes[-1], columns)
    results.append(jnp.concatenate([back[s] for s in range(parts)], axis=2))
    return jnp.concatenate(results, axis=1)


def solution(mesh):
    return jax.shard_map(
        local,
        mesh=mesh,
        in_specs=(
            P("mode", "grid", None),
            P(),
            P(),
            P(),
            P(None, "grid", None),
            P(None, "grid", None),
        ),
        out_specs=P("mode", "grid", None),
        check_vma=False,
    )
```

```python
import jax
import jax.numpy as jnp
from jax import lax
from jax.sharding import PartitionSpec as P


def extended(cells, sides, width):
    for axis, dim in sides:
        count = lax.axis_size(axis)
        ends = count - 1
        head = lax.slice_in_dim(cells, 0, width, axis=dim)
        tail = lax.slice_in_dim(cells, cells.shape[dim] - width, cells.shape[dim], axis=dim)
        cells = jnp.concatenate(
            [
                lax.ppermute(tail, axis, [(i, (i + 1) % count) for i in range(ends)]),
                cells,
                lax.ppermute(head, axis, [((i + 1) % count, i) for i in range(ends)]),
            ],
            axis=dim,
        )
    return cells


def node_terms(padded_field, viscosity, velocity_piece, node_weights):
    field_value = padded_field.astype(jnp.float32)
    center = field_value[:, 1:-1, 1:-1]
    visc_center = viscosity[:, 1:-1, 1:-1]

    def face_flux(near_field, near_visc):
        return 0.5 * (visc_center + near_visc) * (near_field - center)

    north = field_value[:, 2:, 1:-1]
    south = field_value[:, :-2, 1:-1]
    east = field_value[:, 1:-1, 2:]
    west = field_value[:, 1:-1, :-2]
    diffusion = face_flux(north, viscosity[:, 2:, 1:-1]) + face_flux(south, viscosity[:, :-2, 1:-1])
    diffusion = (
        diffusion
        + face_flux(east, viscosity[:, 1:-1, 2:])
        + face_flux(west, viscosity[:, 1:-1, :-2])
    )
    advection = 0.5 * velocity_piece[0] * (north - south) + 0.5 * velocity_piece[1] * (east - west)
    flux = diffusion - advection
    return (node_weights[:, None, None] * flux).astype(jnp.bfloat16)


CHUNKS = 2


def column_chunk(modes_rimmed, first, rows, parts, columns):
    piece = lax.slice_in_dim(modes_rimmed, first, first + rows + 2, axis=1)
    share = piece.shape[0]
    height = rows + 2
    body = piece.reshape(share, height, parts, columns).transpose(2, 0, 1, 3)
    body = body.reshape(parts, share, height * columns)
    place = lax.broadcasted_iota(jnp.int32, (height * columns, columns), 0)
    lane = lax.broadcasted_iota(jnp.int32, (height * columns, columns), 1)
    pick = ((lane < height) & (place == lane * columns + columns - 1)) | (
        (lane >= height) & (lane < 2 * height) & (place == (lane - height) * columns)
    )
    edges = jnp.dot(
        body.reshape(parts * share, height * columns),
        pick.astype(body.dtype),
        preferred_element_type=jnp.float32,
    ).astype(body.dtype).reshape(parts, share, columns)
    zero = jnp.zeros_like(edges[:1])
    from_left = jnp.concatenate([zero, edges[:-1]], axis=0)
    from_right = jnp.concatenate([edges[1:], zero], axis=0)
    side = lax.broadcasted_iota(jnp.int32, edges.shape, 2)
    rims = jnp.where(side < height, from_left, from_right)
    return jnp.concatenate([body, rims], axis=2)


def local(modes_field, chaos_basis, node_weights, node_points, kl_fields, velocity):
    parts = lax.axis_size("mode")
    share, rows, width = modes_field.shape
    columns = width // parts
    lead = rows * 5 // 12
    sizes = [lead, rows - lead]
    starts = [0, lead]
    first_column = lax.axis_index("mode") * columns
    modes_rimmed = extended(modes_field, (("grid", 1),), 1)
    outgoing = [column_chunk(modes_rimmed, f, n, parts, columns) for f, n in zip(starts, sizes)]
    incoming = lax.all_to_all(outgoing[0], "mode", split_axis=0, concat_axis=0, tiled=True)
    kl_fields, incoming = lax.optimization_barrier((kl_fields, incoming))
    kl_rimmed = extended(kl_fields, (("grid", 1),), 1)
    kl_rimmed = jnp.pad(kl_rimmed, ((0, 0), (0, 0), (1, 1)))
    kl_rimmed = lax.dynamic_slice_in_dim(kl_rimmed, first_column, columns + 2, 2)
    velocity_piece = lax.dynamic_slice_in_dim(velocity, first_column, columns, 2)
    viscosity = jnp.exp(
        jnp.einsum("qk,krc->qrc", node_points, kl_rimmed, precision=lax.Precision.HIGHEST)
    )
    result = jnp.zeros(modes_field.shape, modes_field.dtype)
    for chunk, (first, step) in enumerate(zip(starts, sizes)):
        body = (step + 2) * columns
        if chunk > 0:
            incoming = lax.all_to_all(outgoing[chunk], "mode", split_axis=0, concat_axis=0, tiled=True)
            incoming, tendency = lax.optimization_barrier((incoming, tendency))
            back = lax.all_to_all(tendency, "mode", split_axis=0, concat_axis=0, tiled=True)
            back = back.reshape(parts, share, sizes[chunk - 1], columns)
            for s in range(parts):
                result = lax.dynamic_update_slice(result, back[s], (0, starts[chunk - 1], s * columns))
        incoming = incoming.reshape(parts * share, body + columns)
        nodal = jnp.dot(chaos_basis, incoming, preferred_element_type=jnp.float32)
        nodal = nodal.astype(jnp.bfloat16)
        centre = nodal[:, :body].reshape(-1, step + 2, columns)
        west = nodal[:, body : body + step + 2].reshape(-1, step + 2, 1)
        east = nodal[:, body + step + 2 : body + 2 * (step + 2)].reshape(-1, step + 2, 1)
        padded_field = jnp.concatenate([west, centre, east], axis=2)
        visc_piece = lax.slice_in_dim(viscosity, first, first + step + 2, axis=1)
        velocity_rows = lax.slice_in_dim(velocity_piece, first, first + step, axis=1)
        weighted = node_terms(padded_field, visc_piece, velocity_rows, node_weights)
        tendency = jnp.dot(
            chaos_basis.T, weighted.reshape(-1, step * columns), preferred_element_type=jnp.float32
        )
        tendency = tendency.astype(jnp.bfloat16).reshape(parts, share, step * columns)
    back = lax.all_to_all(tendency, "mode", split_axis=0, concat_axis=0, tiled=True)
    back = back.reshape(parts, share, sizes[-1], columns)
    for s in range(parts):
        result = lax.dynamic_update_slice(result, back[s], (0, starts[-1], s * columns))
    return result


def solution(mesh):
    return jax.shard_map(
        local,
        mesh=mesh,
        in_specs=(
            P("mode", "grid", None),
            P(),
            P(),
            P(),
            P(None, "grid", None),
            P(None, "grid", None),
        ),
        out_specs=P("mode", "grid", None),
        check_vma=False,
    )
```

```python
import jax
import jax.numpy as jnp
from jax import lax
from jax.sharding import PartitionSpec as P


def extended(cells, sides, width):
    for axis, dim in sides:
        count = lax.axis_size(axis)
        ends = count - 1
        head = lax.slice_in_dim(cells, 0, width, axis=dim)
        tail = lax.slice_in_dim(cells, cells.shape[dim] - width, cells.shape[dim], axis=dim)
        cells = jnp.concatenate(
            [
                lax.ppermute(tail, axis, [(i, (i + 1) % count) for i in range(ends)]),
                cells,
                lax.ppermute(head, axis, [((i + 1) % count, i) for i in range(ends)]),
            ],
            axis=dim,
        )
    return cells


def node_terms(padded_field, viscosity, velocity_piece, node_weights):
    field_value = padded_field.astype(jnp.float32)
    center = field_value[:, 1:-1, 1:-1]
    visc_center = viscosity[:, 1:-1, 1:-1]

    def face_flux(near_field, near_visc):
        return 0.5 * (visc_center + near_visc) * (near_field - center)

    north = field_value[:, 2:, 1:-1]
    south = field_value[:, :-2, 1:-1]
    east = field_value[:, 1:-1, 2:]
    west = field_value[:, 1:-1, :-2]
    diffusion = face_flux(north, viscosity[:, 2:, 1:-1]) + face_flux(south, viscosity[:, :-2, 1:-1])
    diffusion = (
        diffusion
        + face_flux(east, viscosity[:, 1:-1, 2:])
        + face_flux(west, viscosity[:, 1:-1, :-2])
    )
    advection = 0.5 * velocity_piece[0] * (north - south) + 0.5 * velocity_piece[1] * (east - west)
    flux = diffusion - advection
    return (node_weights[:, None, None] * flux).astype(jnp.bfloat16)


CHUNKS = 2


def column_chunk(modes_rimmed, first, rows, parts, columns):
    piece = lax.slice_in_dim(modes_rimmed, first, first + rows + 2, axis=1)
    share = piece.shape[0]
    height = rows + 2
    body = piece.reshape(share, height, parts, columns).transpose(2, 0, 1, 3)
    body = body.reshape(parts, share, height * columns)
    place = lax.broadcasted_iota(jnp.int32, (height * columns, columns), 0)
    lane = lax.broadcasted_iota(jnp.int32, (height * columns, columns), 1)
    pick = ((lane < height) & (place == lane * columns + columns - 1)) | (
        (lane >= height) & (lane < 2 * height) & (place == (lane - height) * columns)
    )
    edges = jnp.dot(
        body.reshape(parts * share, height * columns),
        pick.astype(body.dtype),
        preferred_element_type=jnp.float32,
    ).astype(body.dtype).reshape(parts, share, columns)
    zero = jnp.zeros_like(edges[:1])
    from_left = jnp.concatenate([zero, edges[:-1]], axis=0)
    from_right = jnp.concatenate([edges[1:], zero], axis=0)
    side = lax.broadcasted_iota(jnp.int32, edges.shape, 2)
    rims = jnp.where(side < height, from_left, from_right)
    return jnp.concatenate([body, rims], axis=2)


def local(modes_field, chaos_basis, node_weights, node_points, kl_fields, velocity):
    parts = lax.axis_size("mode")
    share, rows, width = modes_field.shape
    columns = width // parts
    lead = rows * 7 // 12
    sizes = [lead, rows - lead]
    starts = [0, lead]
    first_column = lax.axis_index("mode") * columns
    modes_rimmed = extended(modes_field, (("grid", 1),), 1)
    outgoing = [column_chunk(modes_rimmed, f, n, parts, columns) for f, n in zip(starts, sizes)]
    incoming = lax.all_to_all(outgoing[0], "mode", split_axis=0, concat_axis=0, tiled=True)
    kl_fields, incoming = lax.optimization_barrier((kl_fields, incoming))
    kl_rimmed = extended(kl_fields, (("grid", 1),), 1)
    kl_rimmed = jnp.pad(kl_rimmed, ((0, 0), (0, 0), (1, 1)))
    kl_rimmed = lax.dynamic_slice_in_dim(kl_rimmed, first_column, columns + 2, 2)
    velocity_piece = lax.dynamic_slice_in_dim(velocity, first_column, columns, 2)
    viscosity = jnp.exp(
        jnp.einsum("qk,krc->qrc", node_points, kl_rimmed, precision=lax.Precision.HIGHEST)
    )
    results = []
    for chunk, (first, step) in enumerate(zip(starts, sizes)):
        body = (step + 2) * columns
        if chunk > 0:
            incoming = lax.all_to_all(outgoing[chunk], "mode", split_axis=0, concat_axis=0, tiled=True)
            incoming, tendency = lax.optimization_barrier((incoming, tendency))
            pending = lax.all_to_all(tendency, "mode", split_axis=0, concat_axis=0, tiled=True)
        incoming = incoming.reshape(parts * share, body + columns)
        nodal = jnp.dot(chaos_basis, incoming, preferred_element_type=jnp.float32)
        nodal = nodal.astype(jnp.bfloat16)
        centre = nodal[:, :body].reshape(-1, step + 2, columns)
        west = nodal[:, body : body + step + 2].reshape(-1, step + 2, 1)
        east = nodal[:, body + step + 2 : body + 2 * (step + 2)].reshape(-1, step + 2, 1)
        padded_field = jnp.concatenate([west, centre, east], axis=2)
        visc_piece = lax.slice_in_dim(viscosity, first, first + step + 2, axis=1)
        velocity_rows = lax.slice_in_dim(velocity_piece, first, first + step, axis=1)
        weighted = node_terms(padded_field, visc_piece, velocity_rows, node_weights)
        tendency = jnp.dot(
            chaos_basis.T, weighted.reshape(-1, step * columns), preferred_element_type=jnp.float32
        )
        tendency = tendency.astype(jnp.bfloat16).reshape(parts, share, step * columns)
    tendency, pending = lax.optimization_barrier((tendency, pending))
    last = lax.all_to_all(tendency, "mode", split_axis=0, concat_axis=0, tiled=True)
    for back, step in ((pending, sizes[0]), (last, sizes[-1])):
        back = back.reshape(parts, share, step, columns)
        results.append(jnp.concatenate([back[s] for s in range(parts)], axis=2))
    return jnp.concatenate(results, axis=1)


def solution(mesh):
    return jax.shard_map(
        local,
        mesh=mesh,
        in_specs=(
            P("mode", "grid", None),
            P(),
            P(),
            P(),
            P(None, "grid", None),
            P(None, "grid", None),
        ),
        out_specs=P("mode", "grid", None),
        check_vma=False,
    )
```

```python
import jax
import jax.numpy as jnp
from jax import lax
from jax.sharding import PartitionSpec as P


def extended(cells, sides, width):
    for axis, dim in sides:
        count = lax.axis_size(axis)
        ends = count - 1
        head = lax.slice_in_dim(cells, 0, width, axis=dim)
        tail = lax.slice_in_dim(cells, cells.shape[dim] - width, cells.shape[dim], axis=dim)
        cells = jnp.concatenate(
            [
                lax.ppermute(tail, axis, [(i, (i + 1) % count) for i in range(ends)]),
                cells,
                lax.ppermute(head, axis, [((i + 1) % count, i) for i in range(ends)]),
            ],
            axis=dim,
        )
    return cells


def node_terms(padded_field, viscosity, velocity_piece, node_weights):
    field_value = padded_field.astype(jnp.float32)
    center = field_value[:, 1:-1, 1:-1]
    visc_center = viscosity[:, 1:-1, 1:-1]

    def face_flux(near_field, near_visc):
        return 0.5 * (visc_center + near_visc) * (near_field - center)

    north = field_value[:, 2:, 1:-1]
    south = field_value[:, :-2, 1:-1]
    east = field_value[:, 1:-1, 2:]
    west = field_value[:, 1:-1, :-2]
    diffusion = face_flux(north, viscosity[:, 2:, 1:-1]) + face_flux(south, viscosity[:, :-2, 1:-1])
    diffusion = (
        diffusion
        + face_flux(east, viscosity[:, 1:-1, 2:])
        + face_flux(west, viscosity[:, 1:-1, :-2])
    )
    advection = 0.5 * velocity_piece[0] * (north - south) + 0.5 * velocity_piece[1] * (east - west)
    flux = diffusion - advection
    return (node_weights[:, None, None] * flux).astype(jnp.bfloat16)


CHUNKS = 2


def column_chunk(modes_rimmed, first, rows, parts, columns):
    piece = lax.slice_in_dim(modes_rimmed, first, first + rows + 2, axis=1)
    share = piece.shape[0]
    height = rows + 2
    body = piece.reshape(share, height, parts, columns).transpose(2, 0, 1, 3)
    body = body.reshape(parts, share, height * columns)
    place = lax.broadcasted_iota(jnp.int32, (height * columns, columns), 0)
    lane = lax.broadcasted_iota(jnp.int32, (height * columns, columns), 1)
    pick = ((lane < height) & (place == lane * columns + columns - 1)) | (
        (lane >= height) & (lane < 2 * height) & (place == (lane - height) * columns)
    )
    edges = jnp.dot(
        body.reshape(parts * share, height * columns),
        pick.astype(body.dtype),
        preferred_element_type=jnp.float32,
    ).astype(body.dtype).reshape(parts, share, columns)
    zero = jnp.zeros_like(edges[:1])
    from_left = jnp.concatenate([zero, edges[:-1]], axis=0)
    from_right = jnp.concatenate([edges[1:], zero], axis=0)
    side = lax.broadcasted_iota(jnp.int32, edges.shape, 2)
    rims = jnp.where(side < height, from_left, from_right)
    return jnp.concatenate([body, rims], axis=2)


def local(modes_field, chaos_basis, node_weights, node_points, kl_fields, velocity):
    parts = lax.axis_size("mode")
    share, rows, width = modes_field.shape
    columns = width // parts
    lead = rows * 11 // 24
    sizes = [lead, rows - lead]
    starts = [0, lead]
    first_column = lax.axis_index("mode") * columns
    modes_rimmed = extended(modes_field, (("grid", 1),), 1)
    outgoing = [column_chunk(modes_rimmed, f, n, parts, columns) for f, n in zip(starts, sizes)]
    incoming = lax.all_to_all(outgoing[0], "mode", split_axis=0, concat_axis=0, tiled=True)
    kl_fields, incoming = lax.optimization_barrier((kl_fields, incoming))
    kl_rimmed = extended(kl_fields, (("grid", 1),), 1)
    kl_rimmed = jnp.pad(kl_rimmed, ((0, 0), (0, 0), (1, 1)))
    kl_rimmed = lax.dynamic_slice_in_dim(kl_rimmed, first_column, columns + 2, 2)
    velocity_piece = lax.dynamic_slice_in_dim(velocity, first_column, columns, 2)
    viscosity = jnp.exp(
        jnp.einsum("qk,krc->qrc", node_points, kl_rimmed, precision=lax.Precision.HIGHEST)
    )
    results = []
    for chunk, (first, step) in enumerate(zip(starts, sizes)):
        body = (step + 2) * columns
        if chunk > 0:
            incoming = lax.all_to_all(outgoing[chunk], "mode", split_axis=0, concat_axis=0, tiled=True)
            incoming, tendency = lax.optimization_barrier((incoming, tendency))
            back = lax.all_to_all(tendency, "mode", split_axis=0, concat_axis=0, tiled=True)
            back = back.reshape(parts, share, sizes[chunk - 1], columns)
            results.append(jnp.concatenate([back[s] for s in range(parts)], axis=2))
        incoming = incoming.reshape(parts * share, body + columns)
        nodal = jnp.dot(chaos_basis, incoming, preferred_element_type=jnp.float32)
        nodal = nodal.astype(jnp.bfloat16)
        centre = nodal[:, :body].reshape(-1, step + 2, columns)
        west = nodal[:, body : body + step + 2].reshape(-1, step + 2, 1)
        east = nodal[:, body + step + 2 : body + 2 * (step + 2)].reshape(-1, step + 2, 1)
        padded_field = jnp.concatenate([west, centre, east], axis=2)
        visc_piece = lax.slice_in_dim(viscosity, first, first + step + 2, axis=1)
        velocity_rows = lax.slice_in_dim(velocity_piece, first, first + step, axis=1)
        weighted = node_terms(padded_field, visc_piece, velocity_rows, node_weights)
        tendency = jnp.dot(
            chaos_basis.T, weighted.reshape(-1, step * columns), preferred_element_type=jnp.float32
        )
        tendency = tendency.astype(jnp.bfloat16).reshape(parts, share, step * columns)
    back = lax.all_to_all(tendency, "mode", split_axis=0, concat_axis=0, tiled=True)
    back = back.reshape(parts, share, sizes[-1], columns)
    results.append(jnp.concatenate([back[s] for s in range(parts)], axis=2))
    return jnp.concatenate(results, axis=1)


def solution(mesh):
    return jax.shard_map(
        local,
        mesh=mesh,
        in_specs=(
            P("mode", "grid", None),
            P(),
            P(),
            P(),
            P(None, "grid", None),
            P(None, "grid", None),
        ),
        out_specs=P("mode", "grid", None),
        check_vma=False,
    )
```

```python
import jax
import jax.numpy as jnp
from jax import lax
from jax.sharding import PartitionSpec as P


def extended(cells, sides, width):
    for axis, dim in sides:
        count = lax.axis_size(axis)
        ends = count - 1
        head = lax.slice_in_dim(cells, 0, width, axis=dim)
        tail = lax.slice_in_dim(cells, cells.shape[dim] - width, cells.shape[dim], axis=dim)
        cells = jnp.concatenate(
            [
                lax.ppermute(tail, axis, [(i, (i + 1) % count) for i in range(ends)]),
                cells,
                lax.ppermute(head, axis, [((i + 1) % count, i) for i in range(ends)]),
            ],
            axis=dim,
        )
    return cells


def node_terms(padded_field, viscosity, velocity_piece, node_weights):
    field_value = padded_field.astype(jnp.float32)
    center = field_value[:, 1:-1, 1:-1]
    visc_center = viscosity[:, 1:-1, 1:-1]

    def face_flux(near_field, near_visc):
        return 0.5 * (visc_center + near_visc) * (near_field - center)

    north = field_value[:, 2:, 1:-1]
    south = field_value[:, :-2, 1:-1]
    east = field_value[:, 1:-1, 2:]
    west = field_value[:, 1:-1, :-2]
    diffusion = face_flux(north, viscosity[:, 2:, 1:-1]) + face_flux(south, viscosity[:, :-2, 1:-1])
    diffusion = (
        diffusion
        + face_flux(east, viscosity[:, 1:-1, 2:])
        + face_flux(west, viscosity[:, 1:-1, :-2])
    )
    advection = 0.5 * velocity_piece[0] * (north - south) + 0.5 * velocity_piece[1] * (east - west)
    flux = diffusion - advection
    return (node_weights[:, None, None] * flux).astype(jnp.bfloat16)


CHUNKS = 2


def column_chunk(modes_rimmed, first, rows, parts, columns):
    piece = lax.slice_in_dim(modes_rimmed, first, first + rows + 2, axis=1)
    share = piece.shape[0]
    height = rows + 2
    body = piece.reshape(share, height, parts, columns).transpose(2, 0, 1, 3)
    body = body.reshape(parts, share, height * columns)
    place = lax.broadcasted_iota(jnp.int32, (height * columns, columns), 0)
    lane = lax.broadcasted_iota(jnp.int32, (height * columns, columns), 1)
    pick = ((lane < height) & (place == lane * columns + columns - 1)) | (
        (lane >= height) & (lane < 2 * height) & (place == (lane - height) * columns)
    )
    edges = jnp.dot(
        body.reshape(parts * share, height * columns),
        pick.astype(body.dtype),
        preferred_element_type=jnp.float32,
    ).astype(body.dtype).reshape(parts, share, columns)
    zero = jnp.zeros_like(edges[:1])
    from_left = jnp.concatenate([zero, edges[:-1]], axis=0)
    from_right = jnp.concatenate([edges[1:], zero], axis=0)
    side = lax.broadcasted_iota(jnp.int32, edges.shape, 2)
    rims = jnp.where(side < height, from_left, from_right)
    return jnp.concatenate([body, rims], axis=2)


def local(modes_field, chaos_basis, node_weights, node_points, kl_fields, velocity):
    parts = lax.axis_size("mode")
    share, rows, width = modes_field.shape
    columns = width // parts
    lead = rows * 11 // 24
    sizes = [lead, rows - lead]
    starts = [0, lead]
    first_column = lax.axis_index("mode") * columns
    modes_rimmed = extended(modes_field, (("grid", 1),), 1)
    outgoing = [column_chunk(modes_rimmed, f, n, parts, columns) for f, n in zip(starts, sizes)]
    incoming = lax.all_to_all(outgoing[0], "mode", split_axis=0, concat_axis=0, tiled=True)
    kl_fields, incoming = lax.optimization_barrier((kl_fields, incoming))
    kl_rimmed = extended(kl_fields, (("grid", 1),), 1)
    kl_rimmed = jnp.pad(kl_rimmed, ((0, 0), (0, 0), (1, 1)))
    kl_rimmed = lax.dynamic_slice_in_dim(kl_rimmed, first_column, columns + 2, 2)
    velocity_piece = lax.dynamic_slice_in_dim(velocity, first_column, columns, 2)
    viscosity = jnp.exp(
        jnp.einsum("qk,krc->qrc", node_points, kl_rimmed, precision=lax.Precision.HIGHEST)
    )
    results = []
    for chunk, (first, step) in enumerate(zip(starts, sizes)):
        body = (step + 2) * columns
        if chunk > 0:
            incoming = lax.all_to_all(outgoing[chunk], "mode", split_axis=0, concat_axis=0, tiled=True)
            incoming, tendency = lax.optimization_barrier((incoming, tendency))
            back = lax.all_to_all(tendency, "mode", split_axis=0, concat_axis=0, tiled=True)
            results.append(back.reshape(parts, share, sizes[chunk - 1], columns))
        incoming = incoming.reshape(parts * share, body + columns)
        nodal = jnp.dot(chaos_basis, incoming, preferred_element_type=jnp.float32)
        nodal = nodal.astype(jnp.bfloat16)
        centre = nodal[:, :body].reshape(-1, step + 2, columns)
        west = nodal[:, body : body + step + 2].reshape(-1, step + 2, 1)
        east = nodal[:, body + step + 2 : body + 2 * (step + 2)].reshape(-1, step + 2, 1)
        padded_field = jnp.concatenate([west, centre, east], axis=2)
        visc_piece = lax.slice_in_dim(viscosity, first, first + step + 2, axis=1)
        velocity_rows = lax.slice_in_dim(velocity_piece, first, first + step, axis=1)
        weighted = node_terms(padded_field, visc_piece, velocity_rows, node_weights)
        tendency = jnp.dot(
            chaos_basis.T, weighted.reshape(-1, step * columns), preferred_element_type=jnp.float32
        )
        tendency = tendency.astype(jnp.bfloat16).reshape(parts, share, step * columns)
    back = lax.all_to_all(tendency, "mode", split_axis=0, concat_axis=0, tiled=True)
    results.append(back.reshape(parts, share, sizes[-1], columns))
    return jnp.concatenate(
        [jnp.concatenate([piece[s] for piece in results], axis=1) for s in range(parts)], axis=2
    )


def solution(mesh):
    return jax.shard_map(
        local,
        mesh=mesh,
        in_specs=(
            P("mode", "grid", None),
            P(),
            P(),
            P(),
            P(None, "grid", None),
            P(None, "grid", None),
        ),
        out_specs=P("mode", "grid", None),
        check_vma=False,
    )
```

```python
import jax
import jax.numpy as jnp
from jax import lax
from jax.sharding import PartitionSpec as P


def extended(cells, sides, width):
    for axis, dim in sides:
        count = lax.axis_size(axis)
        ends = count - 1
        head = lax.slice_in_dim(cells, 0, width, axis=dim)
        tail = lax.slice_in_dim(cells, cells.shape[dim] - width, cells.shape[dim], axis=dim)
        cells = jnp.concatenate(
            [
                lax.ppermute(tail, axis, [(i, (i + 1) % count) for i in range(ends)]),
                cells,
                lax.ppermute(head, axis, [((i + 1) % count, i) for i in range(ends)]),
            ],
            axis=dim,
        )
    return cells


def node_terms(padded_field, viscosity, velocity_piece, node_weights):
    field_value = padded_field.astype(jnp.float32)
    center = field_value[:, 1:-1, 1:-1]
    visc_center = viscosity[:, 1:-1, 1:-1]

    def face_flux(near_field, near_visc):
        return 0.5 * (visc_center + near_visc) * (near_field - center)

    north = field_value[:, 2:, 1:-1]
    south = field_value[:, :-2, 1:-1]
    east = field_value[:, 1:-1, 2:]
    west = field_value[:, 1:-1, :-2]
    diffusion = face_flux(north, viscosity[:, 2:, 1:-1]) + face_flux(south, viscosity[:, :-2, 1:-1])
    diffusion = (
        diffusion
        + face_flux(east, viscosity[:, 1:-1, 2:])
        + face_flux(west, viscosity[:, 1:-1, :-2])
    )
    advection = 0.5 * velocity_piece[0] * (north - south) + 0.5 * velocity_piece[1] * (east - west)
    flux = diffusion - advection
    return (node_weights[:, None, None] * flux).astype(jnp.bfloat16)


CHUNKS = 2


def column_chunk(modes_rimmed, first, rows, parts, columns):
    piece = lax.slice_in_dim(modes_rimmed, first, first + rows + 2, axis=1)
    share = piece.shape[0]
    height = rows + 2
    body = piece.reshape(share, height, parts, columns).transpose(2, 0, 1, 3)
    body = body.reshape(parts, share, height * columns)
    place = lax.broadcasted_iota(jnp.int32, (height * columns, columns), 0)
    lane = lax.broadcasted_iota(jnp.int32, (height * columns, columns), 1)
    pick = ((lane < height) & (place == lane * columns + columns - 1)) | (
        (lane >= height) & (lane < 2 * height) & (place == (lane - height) * columns)
    )
    edges = jnp.dot(
        body.reshape(parts * share, height * columns),
        pick.astype(body.dtype),
        preferred_element_type=jnp.float32,
    ).astype(body.dtype).reshape(parts, share, columns)
    zero = jnp.zeros_like(edges[:1])
    from_left = jnp.concatenate([zero, edges[:-1]], axis=0)
    from_right = jnp.concatenate([edges[1:], zero], axis=0)
    side = lax.broadcasted_iota(jnp.int32, edges.shape, 2)
    rims = jnp.where(side < height, from_left, from_right)
    return jnp.concatenate([body, rims], axis=2)


def local(modes_field, chaos_basis, node_weights, node_points, kl_fields, velocity):
    parts = lax.axis_size("mode")
    share, rows, width = modes_field.shape
    columns = width // parts
    lead = rows * 11 // 24
    sizes = [lead, rows - lead]
    starts = [0, lead]
    first_column = lax.axis_index("mode") * columns
    modes_rimmed = extended(modes_field, (("grid", 1),), 1)
    outgoing = [column_chunk(modes_rimmed, f, n, parts, columns) for f, n in zip(starts, sizes)]
    incoming = lax.all_to_all(outgoing[0], "mode", split_axis=0, concat_axis=0, tiled=True)
    kl_fields, incoming = lax.optimization_barrier((kl_fields, incoming))
    kl_rimmed = extended(kl_fields, (("grid", 1),), 1)
    kl_rimmed = jnp.pad(kl_rimmed, ((0, 0), (0, 0), (1, 1)))
    kl_rimmed = lax.dynamic_slice_in_dim(kl_rimmed, first_column, columns + 2, 2)
    velocity_piece = lax.dynamic_slice_in_dim(velocity, first_column, columns, 2)
    results = []
    for chunk, (first, step) in enumerate(zip(starts, sizes)):
        body = (step + 2) * columns
        kl_piece = lax.slice_in_dim(kl_rimmed, first, first + step + 2, axis=1)
        if chunk > 0:
            incoming = lax.all_to_all(outgoing[chunk], "mode", split_axis=0, concat_axis=0, tiled=True)
            incoming, tendency, kl_piece = lax.optimization_barrier((incoming, tendency, kl_piece))
            back = lax.all_to_all(tendency, "mode", split_axis=0, concat_axis=0, tiled=True)
            results.append(back.reshape(parts, share, sizes[chunk - 1], columns))
        incoming = incoming.reshape(parts * share, body + columns)
        nodal = jnp.dot(chaos_basis, incoming, preferred_element_type=jnp.float32)
        nodal = nodal.astype(jnp.bfloat16)
        centre = nodal[:, :body].reshape(-1, step + 2, columns)
        west = nodal[:, body : body + step + 2].reshape(-1, step + 2, 1)
        east = nodal[:, body + step + 2 : body + 2 * (step + 2)].reshape(-1, step + 2, 1)
        padded_field = jnp.concatenate([west, centre, east], axis=2)
        visc_piece = jnp.exp(
            jnp.einsum("qk,krc->qrc", node_points, kl_piece, precision=lax.Precision.HIGHEST)
        )
        velocity_rows = lax.slice_in_dim(velocity_piece, first, first + step, axis=1)
        weighted = node_terms(padded_field, visc_piece, velocity_rows, node_weights)
        tendency = jnp.dot(
            chaos_basis.T, weighted.reshape(-1, step * columns), preferred_element_type=jnp.float32
        )
        tendency = tendency.astype(jnp.bfloat16).reshape(parts, share, step * columns)
    back = lax.all_to_all(tendency, "mode", split_axis=0, concat_axis=0, tiled=True)
    results.append(back.reshape(parts, share, sizes[-1], columns))
    return jnp.concatenate(
        [jnp.concatenate([piece[s] for piece in results], axis=1) for s in range(parts)], axis=2
    )


def solution(mesh):
    return jax.shard_map(
        local,
        mesh=mesh,
        in_specs=(
            P("mode", "grid", None),
            P(),
            P(),
            P(),
            P(None, "grid", None),
            P(None, "grid", None),
        ),
        out_specs=P("mode", "grid", None),
        check_vma=False,
    )
```

```python
import jax
import jax.numpy as jnp
from jax import lax
from jax.sharding import PartitionSpec as P


def extended(cells, sides, width):
    for axis, dim in sides:
        count = lax.axis_size(axis)
        ends = count - 1
        head = lax.slice_in_dim(cells, 0, width, axis=dim)
        tail = lax.slice_in_dim(cells, cells.shape[dim] - width, cells.shape[dim], axis=dim)
        cells = jnp.concatenate(
            [
                lax.ppermute(tail, axis, [(i, (i + 1) % count) for i in range(ends)]),
                cells,
                lax.ppermute(head, axis, [((i + 1) % count, i) for i in range(ends)]),
            ],
            axis=dim,
        )
    return cells


def node_terms(padded_field, viscosity, velocity_piece, node_weights):
    field_value = padded_field.astype(jnp.float32)
    center = field_value[:, 1:-1, 1:-1]
    visc_center = viscosity[:, 1:-1, 1:-1]

    def face_flux(near_field, near_visc):
        return 0.5 * (visc_center + near_visc) * (near_field - center)

    north = field_value[:, 2:, 1:-1]
    south = field_value[:, :-2, 1:-1]
    east = field_value[:, 1:-1, 2:]
    west = field_value[:, 1:-1, :-2]
    diffusion = face_flux(north, viscosity[:, 2:, 1:-1]) + face_flux(south, viscosity[:, :-2, 1:-1])
    diffusion = (
        diffusion
        + face_flux(east, viscosity[:, 1:-1, 2:])
        + face_flux(west, viscosity[:, 1:-1, :-2])
    )
    advection = 0.5 * velocity_piece[0] * (north - south) + 0.5 * velocity_piece[1] * (east - west)
    flux = diffusion - advection
    return (node_weights[:, None, None] * flux).astype(jnp.bfloat16)


CHUNKS = 2


def column_chunk(modes_rimmed, first, rows, parts, columns):
    piece = lax.slice_in_dim(modes_rimmed, first, first + rows + 2, axis=1)
    share = piece.shape[0]
    height = rows + 2
    body = piece.reshape(share, height, parts, columns).transpose(2, 0, 1, 3)
    body = body.reshape(parts, share, height * columns)
    place = lax.broadcasted_iota(jnp.int32, (height * columns, columns), 0)
    lane = lax.broadcasted_iota(jnp.int32, (height * columns, columns), 1)
    pick = ((lane < height) & (place == lane * columns + columns - 1)) | (
        (lane >= height) & (lane < 2 * height) & (place == (lane - height) * columns)
    )
    edges = jnp.dot(
        body.reshape(parts * share, height * columns),
        pick.astype(body.dtype),
        preferred_element_type=jnp.float32,
    ).astype(body.dtype).reshape(parts, share, columns)
    zero = jnp.zeros_like(edges[:1])
    from_left = jnp.concatenate([zero, edges[:-1]], axis=0)
    from_right = jnp.concatenate([edges[1:], zero], axis=0)
    side = lax.broadcasted_iota(jnp.int32, edges.shape, 2)
    rims = jnp.where(side < height, from_left, from_right)
    return jnp.concatenate([body, rims], axis=2)


def local(modes_field, chaos_basis, node_weights, node_points, kl_fields, velocity):
    parts = lax.axis_size("mode")
    share, rows, width = modes_field.shape
    columns = width // parts
    lead = rows * 23 // 48
    sizes = [lead, rows - lead]
    starts = [0, lead]
    first_column = lax.axis_index("mode") * columns
    modes_rimmed = extended(modes_field, (("grid", 1),), 1)
    outgoing = [column_chunk(modes_rimmed, f, n, parts, columns) for f, n in zip(starts, sizes)]
    incoming = lax.all_to_all(outgoing[0], "mode", split_axis=0, concat_axis=0, tiled=True)
    kl_fields, incoming = lax.optimization_barrier((kl_fields, incoming))
    kl_rimmed = extended(kl_fields, (("grid", 1),), 1)
    kl_rimmed = jnp.pad(kl_rimmed, ((0, 0), (0, 0), (1, 1)))
    kl_rimmed = lax.dynamic_slice_in_dim(kl_rimmed, first_column, columns + 2, 2)
    velocity_piece = lax.dynamic_slice_in_dim(velocity, first_column, columns, 2)
    viscosity = jnp.exp(
        jnp.einsum("qk,krc->qrc", node_points, kl_rimmed, precision=lax.Precision.HIGHEST)
    )
    results = []
    for chunk, (first, step) in enumerate(zip(starts, sizes)):
        body = (step + 2) * columns
        if chunk > 0:
            incoming = lax.all_to_all(outgoing[chunk], "mode", split_axis=0, concat_axis=0, tiled=True)
            incoming, tendency = lax.optimization_barrier((incoming, tendency))
            back = lax.all_to_all(tendency, "mode", split_axis=0, concat_axis=0, tiled=True)
            results.append(back.reshape(parts, share, sizes[chunk - 1], columns))
        incoming = incoming.reshape(parts * share, body + columns)
        nodal = jnp.dot(chaos_basis, incoming, preferred_element_type=jnp.float32)
        nodal = nodal.astype(jnp.bfloat16)
        centre = nodal[:, :body].reshape(-1, step + 2, columns)
        west = nodal[:, body : body + step + 2].reshape(-1, step + 2, 1)
        east = nodal[:, body + step + 2 : body + 2 * (step + 2)].reshape(-1, step + 2, 1)
        padded_field = jnp.concatenate([west, centre, east], axis=2)
        visc_piece = lax.slice_in_dim(viscosity, first, first + step + 2, axis=1)
        velocity_rows = lax.slice_in_dim(velocity_piece, first, first + step, axis=1)
        weighted = node_terms(padded_field, visc_piece, velocity_rows, node_weights)
        tendency = jnp.dot(
            chaos_basis.T, weighted.reshape(-1, step * columns), preferred_element_type=jnp.float32
        )
        tendency = tendency.astype(jnp.bfloat16).reshape(parts, share, step * columns)
    back = lax.all_to_all(tendency, "mode", split_axis=0, concat_axis=0, tiled=True)
    results.append(back.reshape(parts, share, sizes[-1], columns))
    return jnp.concatenate(
        [jnp.concatenate([piece[s] for piece in results], axis=1) for s in range(parts)], axis=2
    )


def solution(mesh):
    return jax.shard_map(
        local,
        mesh=mesh,
        in_specs=(
            P("mode", "grid", None),
            P(),
            P(),
            P(),
            P(None, "grid", None),
            P(None, "grid", None),
        ),
        out_specs=P("mode", "grid", None),
        check_vma=False,
    )
```

```python
import jax
import jax.numpy as jnp
from jax import lax
from jax.sharding import PartitionSpec as P


def extended(cells, sides, width):
    for axis, dim in sides:
        count = lax.axis_size(axis)
        ends = count - 1
        head = lax.slice_in_dim(cells, 0, width, axis=dim)
        tail = lax.slice_in_dim(cells, cells.shape[dim] - width, cells.shape[dim], axis=dim)
        cells = jnp.concatenate(
            [
                lax.ppermute(tail, axis, [(i, (i + 1) % count) for i in range(ends)]),
                cells,
                lax.ppermute(head, axis, [((i + 1) % count, i) for i in range(ends)]),
            ],
            axis=dim,
        )
    return cells


def node_terms(padded_field, viscosity, velocity_piece, node_weights):
    field_value = padded_field.astype(jnp.float32)
    center = field_value[:, 1:-1, 1:-1]
    visc_center = viscosity[:, 1:-1, 1:-1]

    def face_flux(near_field, near_visc):
        return 0.5 * (visc_center + near_visc) * (near_field - center)

    north = field_value[:, 2:, 1:-1]
    south = field_value[:, :-2, 1:-1]
    east = field_value[:, 1:-1, 2:]
    west = field_value[:, 1:-1, :-2]
    diffusion = face_flux(north, viscosity[:, 2:, 1:-1]) + face_flux(south, viscosity[:, :-2, 1:-1])
    diffusion = (
        diffusion
        + face_flux(east, viscosity[:, 1:-1, 2:])
        + face_flux(west, viscosity[:, 1:-1, :-2])
    )
    advection = 0.5 * velocity_piece[0] * (north - south) + 0.5 * velocity_piece[1] * (east - west)
    flux = diffusion - advection
    return (node_weights[:, None, None] * flux).astype(jnp.bfloat16)


CHUNKS = 2


def column_chunk(modes_rimmed, first, rows, parts, columns):
    piece = lax.slice_in_dim(modes_rimmed, first, first + rows + 2, axis=1)
    share = piece.shape[0]
    height = rows + 2
    body = piece.reshape(share, height, parts, columns).transpose(2, 0, 1, 3)
    body = body.reshape(parts, share, height * columns)
    place = lax.broadcasted_iota(jnp.int32, (height * columns, columns), 0)
    lane = lax.broadcasted_iota(jnp.int32, (height * columns, columns), 1)
    pick = ((lane < height) & (place == lane * columns + columns - 1)) | (
        (lane >= height) & (lane < 2 * height) & (place == (lane - height) * columns)
    )
    edges = jnp.dot(
        body.reshape(parts * share, height * columns),
        pick.astype(body.dtype),
        preferred_element_type=jnp.float32,
    ).astype(body.dtype).reshape(parts, share, columns)
    zero = jnp.zeros_like(edges[:1])
    from_left = jnp.concatenate([zero, edges[:-1]], axis=0)
    from_right = jnp.concatenate([edges[1:], zero], axis=0)
    side = lax.broadcasted_iota(jnp.int32, edges.shape, 2)
    rims = jnp.where(side < height, from_left, from_right)
    return jnp.concatenate([body, rims], axis=2)


def local(modes_field, chaos_basis, node_weights, node_points, kl_fields, velocity):
    parts = lax.axis_size("mode")
    share, rows, width = modes_field.shape
    columns = width // parts
    lead = rows * 7 // 16
    sizes = [lead, rows - lead]
    starts = [0, lead]
    first_column = lax.axis_index("mode") * columns
    modes_rimmed = extended(modes_field, (("grid", 1),), 1)
    outgoing = [column_chunk(modes_rimmed, f, n, parts, columns) for f, n in zip(starts, sizes)]
    incoming = lax.all_to_all(outgoing[0], "mode", split_axis=0, concat_axis=0, tiled=True)
    kl_fields, incoming = lax.optimization_barrier((kl_fields, incoming))
    kl_rimmed = extended(kl_fields, (("grid", 1),), 1)
    kl_rimmed = jnp.pad(kl_rimmed, ((0, 0), (0, 0), (1, 1)))
    kl_rimmed = lax.dynamic_slice_in_dim(kl_rimmed, first_column, columns + 2, 2)
    velocity_piece = lax.dynamic_slice_in_dim(velocity, first_column, columns, 2)
    viscosity = jnp.exp(
        jnp.einsum("qk,krc->qrc", node_points, kl_rimmed, precision=lax.Precision.HIGHEST)
    )
    results = []
    for chunk, (first, step) in enumerate(zip(starts, sizes)):
        body = (step + 2) * columns
        if chunk > 0:
            incoming = lax.all_to_all(outgoing[chunk], "mode", split_axis=0, concat_axis=0, tiled=True)
            incoming, tendency = lax.optimization_barrier((incoming, tendency))
            back = lax.all_to_all(tendency, "mode", split_axis=0, concat_axis=0, tiled=True)
            results.append(back.reshape(parts, share, sizes[chunk - 1], columns))
        incoming = incoming.reshape(parts * share, body + columns)
        nodal = jnp.dot(chaos_basis, incoming, preferred_element_type=jnp.float32)
        nodal = nodal.astype(jnp.bfloat16)
        centre = nodal[:, :body].reshape(-1, step + 2, columns)
        west = nodal[:, body : body + step + 2].reshape(-1, step + 2, 1)
        east = nodal[:, body + step + 2 : body + 2 * (step + 2)].reshape(-1, step + 2, 1)
        padded_field = jnp.concatenate([west, centre, east], axis=2)
        visc_piece = lax.slice_in_dim(viscosity, first, first + step + 2, axis=1)
        velocity_rows = lax.slice_in_dim(velocity_piece, first, first + step, axis=1)
        weighted = node_terms(padded_field, visc_piece, velocity_rows, node_weights)
        tendency = jnp.dot(
            chaos_basis.T, weighted.reshape(-1, step * columns), preferred_element_type=jnp.float32
        )
        tendency = tendency.astype(jnp.bfloat16).reshape(parts, share, step * columns)
    back = lax.all_to_all(tendency, "mode", split_axis=0, concat_axis=0, tiled=True)
    results.append(back.reshape(parts, share, sizes[-1], columns))
    return jnp.concatenate(
        [jnp.concatenate([piece[s] for piece in results], axis=1) for s in range(parts)], axis=2
    )


def solution(mesh):
    return jax.shard_map(
        local,
        mesh=mesh,
        in_specs=(
            P("mode", "grid", None),
            P(),
            P(),
            P(),
            P(None, "grid", None),
            P(None, "grid", None),
        ),
        out_specs=P("mode", "grid", None),
        check_vma=False,
    )
```
